128 devices in a mesh: grains: 128 (over z, x, y, core).
Axes of the slice: x: 4, y: 4, z: 4, core: 2. Of those that a mesh axis runs over, the one named last changes fastest.
Arguments:
- tangent: float32 [8192, 128, 128], P('grains'), may hold values from -48 to 48
- blocks: bfloat16 [8192, 8, 128, 128], P('grains'), may hold values from -0.1875 to 0.1875
- columns: int32 [8192, 8], P('grains'), may hold values from 0 to 95, as said below
- counts: int32 [128], P('grains'), may hold values from 32 to 64, as said below
- send_lists: int32 [128, 2, 16], P('grains'), may hold values from 0 to 63, as said below
Outputs:
- basis: float32 [8192, 128, 128], P('grains')
- r_factor: float32 [128, 128], replicated
The draws below stay inside these ranges and needn't reach their ends.
Inputs may be any that keep to these rules, and one draw needn't show every extreme that they name: `counts`: some device has exactly 64 live block rows; every device has at least 32. Every entry of send_lists[d] is below counts[d]. For block row b of device d, columns[., 0] is b; every other entry is below counts[d] or lies in 64 to 64 + 2 * 16 - 1 (received rows). Entries of slots that are not live follow the same law.
All inputs are finite; a program needn't handle non-finite values.
Results may differ from the reference program's by a relative error of at most 0.0028.
Values may be sent and summed in bfloat16 or wider, within the bound.
No kernel may reach another device: no remote copies, remote signals or barrier semaphores. Data moves between devices by JAX's collectives and lax.ppermute only.
A program may use at most 128 MiB of HBM per device.

```python
import jax
import jax.numpy as jnp
from jax import lax

BR = 64
B = 128
K = 128
NNZ = 8
H = 16
SUBSTEPS = 3
ROWS = 8192
N_GRAINS = 128


def shared_layout(key):
    base = jax.random.fold_in(key, 7)
    sizes = jax.random.randint(jax.random.fold_in(base, 1), (N_GRAINS,), BR // 2, BR + 1)
    chosen = jax.random.randint(jax.random.fold_in(base, 2), (), 0, N_GRAINS)
    device_ids = jnp.arange(N_GRAINS, dtype=jnp.int32)
    sizes = jnp.where(device_ids == chosen, BR, sizes).astype(jnp.int32)
    sends = jax.random.randint(jax.random.fold_in(base, 3), (N_GRAINS, 2, H), 0, sizes[:, None, None])
    sends = sends.at[chosen, 0, 0].set(BR - 1)
    sends = sends.at[chosen, 1, 0].set(0)
    raw = jax.random.randint(jax.random.fold_in(base, 4), (N_GRAINS, BR, NNZ), 0, sizes[:, None, None] + 2 * H)
    mapped = jnp.where(raw < sizes[:, None, None], raw, raw - sizes[:, None, None] + BR)
    own = jnp.broadcast_to(jnp.arange(BR, dtype=jnp.int32)[None, :], (N_GRAINS, BR))
    mapped = mapped.at[:, :, 0].set(own)
    mapped = mapped.at[chosen, 0, 1].set(BR + 2 * H - 1)
    return (sizes, sends.astype(jnp.int32), mapped.reshape(N_GRAINS * BR, NNZ).astype(jnp.int32))


def draw_counts(key, part):
    return shared_layout(key)[0]


def draw_send_lists(key, part):
    return shared_layout(key)[1]


def draw_columns(key, part):
    return shared_layout(key)[2]


def draw_tangent(key, part):
    position = jnp.arange(N_GRAINS * BR, dtype=jnp.float32) // BR / max(N_GRAINS - 1, 1)
    noise = jnp.clip(jax.random.normal(jax.random.fold_in(key, 11), (N_GRAINS * BR, B, K), jnp.float32), -6.0, 6.0)
    scales = jnp.exp(jnp.log(4.0) * position)
    return (noise * scales[:, None, None]).astype(jnp.float32)


def levels(rng, dims, split, least, largest):
    gain, own = 1.0, jax.random.fold_in(rng, 6)
    for dim, parts in split:
        heights = jnp.exp(jax.random.uniform(jax.random.fold_in(own, dim), (parts,), jnp.float32, least / len(split), largest / len(split)))
        gain = gain * jnp.repeat(heights, dims[dim] // parts).reshape([-1 if axis == dim else 1 for axis in range(len(dims))])
    return gain


def gaussian(own_key, extent, deviation, limit, shards=(), held_as=jnp.bfloat16):
    drawn = jax.random.normal(own_key, extent, jnp.float32) * deviation
    if len(shards) > 0:
        drawn = levels(own_key, extent, shards, -0.22, 0.18) * drawn
    return jnp.clip(drawn, min=-limit, max=limit).astype(held_as)


def setup_inputs(seed: int = 0) -> dict:
    streams_of = jax.random.split(jax.random.key(seed), 6)
    tangent = draw_tangent(jax.random.fold_in(streams_of[5], 71), 0)
    blocks = gaussian(streams_of[1], (ROWS, NNZ, B, B), (B * NNZ) ** -0.5, 0.1875, ((0, 128),))
    columns = draw_columns(jax.random.fold_in(streams_of[5], 71), 0)
    counts = draw_counts(jax.random.fold_in(streams_of[5], 71), 0)
    send_lists = draw_send_lists(jax.random.fold_in(streams_of[5], 71), 0)
    return {"tangent": tangent, "blocks": blocks, "columns": columns, "counts": counts, "send_lists": send_lists}


def pick_rows(rounded, indices):
    return rounded[indices]

def propagate(args):
    extended, cols, blk = args
    gathered = extended[cols]
    return jnp.einsum('bkij,bkjv->biv', blk.astype(jnp.float32), gathered.astype(jnp.float32), precision=lax.Precision.HIGHEST)

def reference(tangent, blocks, columns, counts, send_lists):
    live = (jnp.arange(BR, dtype=jnp.int32)[None, :] < counts[:, None]).astype(jnp.float32)
    mask = live.reshape(N_GRAINS * BR, 1, 1)
    state = tangent * mask
    cols = columns.reshape(N_GRAINS, BR, NNZ)
    blk = blocks.reshape(N_GRAINS, BR, NNZ, B, B)
    for step in range(SUBSTEPS):
        rounded = state.astype(jnp.bfloat16).reshape(N_GRAINS, BR, B, K)
        to_lower = jax.vmap(pick_rows)(rounded, send_lists[:, 0])
        to_upper = jax.vmap(pick_rows)(rounded, send_lists[:, 1])
        from_lower = jnp.roll(to_upper, 1, axis=0)
        from_upper = jnp.roll(to_lower, -1, axis=0)
        extended = jnp.concatenate([rounded, from_lower, from_upper], axis=1)
        update = lax.map(propagate, (extended, cols, blk)).reshape(N_GRAINS * BR, B, K)
        state = state + update * mask
    flat = state.reshape(N_GRAINS * BR * B, K)
    q_full, r_full = jnp.linalg.qr(flat)
    signs = jnp.sign(jnp.diagonal(r_full))
    basis = (q_full * signs[None, :]).reshape(N_GRAINS * BR, B, K)
    return (basis, r_full * signs[:, None])
```

```python
import jax
import jax.numpy as jnp
from jax import lax
from jax.sharding import PartitionSpec as P

SUBSTEPS = 3


def passed_along(shard, axis, by):
    length = lax.axis_size(axis)
    return lax.ppermute(shard, axis, [(i, (i + by) % length) for i in range(length)])


def tree_sum(value, axis):
    length = lax.axis_size(axis)
    distance = 1
    while distance < length:
        partner = [(i, i ^ distance) for i in range(length)]
        value = value + lax.ppermute(value, axis, partner)
        distance *= 2
    return value


def apply_inverse(matrix, lower):
    return lax.linalg.triangular_solve(lower, matrix, left_side=False, lower=True, transpose_a=True)


def local(tangent, blocks, columns, counts, send_lists):
    slots, width, vectors = tangent.shape
    live = (jnp.arange(slots, dtype=jnp.int32) < counts[0]).astype(jnp.float32)[:, None, None]
    state = tangent * live
    for step in range(SUBSTEPS):
        rounded = state.astype(jnp.bfloat16)
        to_lower = rounded[send_lists[0, 0]]
        to_upper = rounded[send_lists[0, 1]]
        from_lower = passed_along(to_upper, "grains", 1)
        from_upper = passed_along(to_lower, "grains", -1)
        extended = jnp.concatenate([rounded, from_lower, from_upper], axis=0)
        gathered = extended[columns]
        update = jnp.einsum("bkij,bkjv->biv", blocks, gathered, preferred_element_type=jnp.float32)
        state = state + update * live
    flat = state.reshape(slots * width, vectors)
    first_low = jnp.linalg.cholesky(
        tree_sum(jnp.einsum("rk,rv->kv", flat, flat, precision=lax.Precision.HIGHEST), "grains")
    )
    basis = apply_inverse(flat, first_low)
    r_factor = first_low.T
    return (basis.reshape(slots, width, vectors), r_factor)


def solution(mesh):
    in_specs = (
        P("grains", None, None),
        P("grains", None, None, None),
        P("grains", None),
        P("grains"),
        P("grains", None, None),
    )
    out_specs = (P("grains", None, None), P())
    return jax.shard_map(local, mesh=mesh, in_specs=in_specs, out_specs=out_specs, check_vma=False)
```

```python
import functools

import jax
import jax.numpy as jnp
from jax import lax
from jax.experimental import pallas as pl
from jax.experimental.pallas import tpu as pltpu
from jax.sharding import PartitionSpec as P

SUBSTEPS = 3
ROWS_PER_STEP = 4


def passed_along(shard, axis, by):
    length = lax.axis_size(axis)
    return lax.ppermute(shard, axis, [(i, (i + by) % length) for i in range(length)])


def tree_sum(value, axis):
    length = lax.axis_size(axis)
    distance = 1
    while distance < length:
        partner = [(i, i ^ distance) for i in range(length)]
        value = value + lax.ppermute(value, axis, partner)
        distance *= 2
    return value


def substep_kernel(cols_ref, count_ref, own_hbm, low_hbm, high_hbm, blocks_ref, state_ref,
                   new_state_ref, new_rounded_ref, extended, sems, *, nnz, per_step):
    step = pl.program_id(0)
    slots = own_hbm.shape[0]
    halo = low_hbm.shape[0]

    @pl.when(step == 0)
    def _():
        copies = [
            pltpu.make_async_copy(own_hbm, extended.at[pl.ds(0, slots)], sems.at[0]),
            pltpu.make_async_copy(low_hbm, extended.at[pl.ds(slots, halo)], sems.at[1]),
            pltpu.make_async_copy(high_hbm, extended.at[pl.ds(slots + halo, halo)], sems.at[2]),
        ]
        for copy in copies:
            copy.start()
        for copy in copies:
            copy.wait()

    count = count_ref[0]
    for r in range(per_step):
        row = step * per_step + r
        acc = jnp.zeros(state_ref.shape[1:], jnp.float32)
        for k in range(nnz):
            col = cols_ref[row * nnz + k]
            acc = acc + jnp.dot(blocks_ref[r, k], extended[col], preferred_element_type=jnp.float32)
        new = state_ref[r] + jnp.where(row < count, acc, 0.0)
        new_state_ref[r] = new
        new_rounded_ref[r] = new.astype(jnp.bfloat16)


def substep(cols, count, rounded, from_lower, from_upper, blocks, state):
    slots, width, vectors = state.shape
    nnz = blocks.shape[1]
    halo = from_lower.shape[0]
    per_step = ROWS_PER_STEP
    kernel = functools.partial(substep_kernel, nnz=nnz, per_step=per_step)
    grid_spec = pltpu.PrefetchScalarGridSpec(
        num_scalar_prefetch=2,
        grid=(slots // per_step,),
        in_specs=[
            pl.BlockSpec(memory_space=pl.ANY),
            pl.BlockSpec(memory_space=pl.ANY),
            pl.BlockSpec(memory_space=pl.ANY),
            pl.BlockSpec((per_step, nnz, width, width), lambda i, c, n: (i, 0, 0, 0)),
            pl.BlockSpec((per_step, width, vectors), lambda i, c, n: (i, 0, 0)),
        ],
        out_specs=[
            pl.BlockSpec((per_step, width, vectors), lambda i, c, n: (i, 0, 0)),
            pl.BlockSpec((per_step, width, vectors), lambda i, c, n: (i, 0, 0)),
        ],
        scratch_shapes=[
            pltpu.VMEM((slots + 2 * halo, width, vectors), jnp.bfloat16),
            pltpu.SemaphoreType.DMA((3,)),
        ],
    )
    return pl.pallas_call(
        kernel,
        grid_spec=grid_spec,
        out_shape=[
            jax.ShapeDtypeStruct(state.shape, jnp.float32),
            jax.ShapeDtypeStruct(state.shape, jnp.bfloat16),
        ],
        compiler_params=pltpu.CompilerParams(dimension_semantics=("arbitrary",)),
    )(cols, count, rounded, from_lower, from_upper, blocks, state)


def local(tangent, blocks, columns, counts, send_lists):
    slots, width, vectors = tangent.shape
    live = (jnp.arange(slots, dtype=jnp.int32) < counts[0]).astype(jnp.float32)[:, None, None]
    state = tangent * live
    rounded = state.astype(jnp.bfloat16)
    cols = columns.reshape(-1)
    for step in range(SUBSTEPS):
        to_lower = rounded[send_lists[0, 0]]
        to_upper = rounded[send_lists[0, 1]]
        from_lower = passed_along(to_upper, "grains", 1)
        from_upper = passed_along(to_lower, "grains", -1)
        state, rounded = substep(cols, counts, rounded, from_lower, from_upper, blocks, state)
    flat = state.reshape(slots * width, vectors)
    first_low = jnp.linalg.cholesky(
        tree_sum(jnp.einsum("rk,rv->kv", flat, flat, precision=lax.Precision.HIGHEST), "grains")
    )
    basis = lax.linalg.triangular_solve(first_low, flat, left_side=False, lower=True, transpose_a=True)
    r_factor = first_low.T
    return (basis.reshape(slots, width, vectors), r_factor)


def solution(mesh):
    in_specs = (
        P("grains", None, None),
        P("grains", None, None, None),
        P("grains", None),
        P("grains"),
        P("grains", None, None),
    )
    out_specs = (P("grains", None, None), P())
    return jax.shard_map(local, mesh=mesh, in_specs=in_specs, out_specs=out_specs, check_vma=False)
```

```python
import functools

import jax
import jax.numpy as jnp
from jax import lax
from jax.experimental import pallas as pl
from jax.experimental.pallas import tpu as pltpu
from jax.sharding import PartitionSpec as P

SUBSTEPS = 3
ROWS_PER_STEP = 16


def passed_along(shard, axis, by):
    length = lax.axis_size(axis)
    return lax.ppermute(shard, axis, [(i, (i + by) % length) for i in range(length)])


def tree_sum(value, axis):
    length = lax.axis_size(axis)
    distance = 1
    while distance < length:
        partner = [(i, i ^ distance) for i in range(length)]
        value = value + lax.ppermute(value, axis, partner)
        distance *= 2
    return value


def substep_kernel(cols_ref, count_ref, own_hbm, low_hbm, high_hbm, blocks_ref, state_ref,
                   new_state_ref, out_ref, extended, sems, *, nnz, per_step, last):
    step = pl.program_id(0)
    slots = own_hbm.shape[0]
    halo = low_hbm.shape[0]

    @pl.when(step == 0)
    def _():
        copies = [
            pltpu.make_async_copy(own_hbm, extended.at[pl.ds(0, slots)], sems.at[0]),
            pltpu.make_async_copy(low_hbm, extended.at[pl.ds(slots, halo)], sems.at[1]),
            pltpu.make_async_copy(high_hbm, extended.at[pl.ds(slots + halo, halo)], sems.at[2]),
        ]
        for copy in copies:
            copy.start()
        for copy in copies:
            copy.wait()

    count = count_ref[0]
    for r in range(per_step):
        row = step * per_step + r
        acc = jnp.zeros(state_ref.shape[1:], jnp.float32)
        for k in range(nnz):
            col = cols_ref[row * nnz + k]
            acc = acc + jnp.dot(blocks_ref[r, k], extended[col], preferred_element_type=jnp.float32)
        new = state_ref[r] + jnp.where(row < count, acc, 0.0)
        new_state_ref[r] = new
        if not last:
            out_ref[r] = new.astype(jnp.bfloat16)
            continue
        part = lax.dot_general(new, new, (((0,), (0,)), ((), ())), precision=lax.Precision.HIGHEST,
                               preferred_element_type=jnp.float32)
        if r == 0:
            @pl.when(step == 0)
            def _():
                out_ref[...] = jnp.zeros_like(out_ref)
        out_ref[...] += part


def substep(cols, count, rounded, from_lower, from_upper, blocks, state, last):
    slots, width, vectors = state.shape
    nnz = blocks.shape[1]
    halo = from_lower.shape[0]
    per_step = ROWS_PER_STEP
    kernel = functools.partial(substep_kernel, nnz=nnz, per_step=per_step, last=last)
    grid_spec = pltpu.PrefetchScalarGridSpec(
        num_scalar_prefetch=2,
        grid=(slots // per_step,),
        in_specs=[
            pl.BlockSpec(memory_space=pl.ANY),
            pl.BlockSpec(memory_space=pl.ANY),
            pl.BlockSpec(memory_space=pl.ANY),
            pl.BlockSpec((per_step, nnz, width, width), lambda i, c, n: (i, 0, 0, 0)),
            pl.BlockSpec((per_step, width, vectors), lambda i, c, n: (i, 0, 0)),
        ],
        out_specs=[
            pl.BlockSpec((per_step, width, vectors), lambda i, c, n: (i, 0, 0)),
            pl.BlockSpec((vectors, vectors), lambda i, c, n: (0, 0)) if last
            else pl.BlockSpec((per_step, width, vectors), lambda i, c, n: (i, 0, 0)),
        ],
        scratch_shapes=[
            pltpu.VMEM((slots + 2 * halo, width, vectors), jnp.bfloat16),
            pltpu.SemaphoreType.DMA((3,)),
        ],
    )
    return pl.pallas_call(
        kernel,
        grid_spec=grid_spec,
        out_shape=[
            jax.ShapeDtypeStruct(state.shape, jnp.float32),
            jax.ShapeDtypeStruct((vectors, vectors), jnp.float32) if last
            else jax.ShapeDtypeStruct(state.shape, jnp.bfloat16),
        ],
        compiler_params=pltpu.CompilerParams(dimension_semantics=("arbitrary",)),
    )(cols, count, rounded, from_lower, from_upper, blocks, state)


def local(tangent, blocks, columns, counts, send_lists):
    slots, width, vectors = tangent.shape
    live = (jnp.arange(slots, dtype=jnp.int32) < counts[0]).astype(jnp.float32)[:, None, None]
    state = tangent * live
    rounded = state.astype(jnp.bfloat16)
    cols = columns.reshape(-1)
    for step in range(SUBSTEPS):
        to_lower = rounded[send_lists[0, 0]]
        to_upper = rounded[send_lists[0, 1]]
        from_lower = passed_along(to_upper, "grains", 1)
        from_upper = passed_along(to_lower, "grains", -1)
        state, rounded = substep(cols, counts, rounded, from_lower, from_upper, blocks, state,
                                 step == SUBSTEPS - 1)
    gram = rounded
    flat = state.reshape(slots * width, vectors)
    first_low = jnp.linalg.cholesky(tree_sum(gram, "grains"))
    inverse = lax.linalg.triangular_solve(
        first_low, jnp.eye(vectors, dtype=jnp.float32), left_side=True, lower=True
    )
    basis = jnp.dot(flat, inverse.T, precision=lax.Precision.HIGHEST)
    r_factor = first_low.T
    return (basis.reshape(slots, width, vectors), r_factor)


def solution(mesh):
    in_specs = (
        P("grains", None, None),
        P("grains", None, None, None),
        P("grains", None),
        P("grains"),
        P("grains", None, None),
    )
    out_specs = (P("grains", None, None), P())
    return jax.shard_map(local, mesh=mesh, in_specs=in_specs, out_specs=out_specs, check_vma=False)
```

```python
import functools

import jax
import jax.numpy as jnp
from jax import lax
from jax.experimental import pallas as pl
from jax.experimental.pallas import tpu as pltpu
from jax.sharding import PartitionSpec as P

SUBSTEPS = 3
ROWS_PER_STEP = 16


def passed_along(shard, axis, by):
    length = lax.axis_size(axis)
    return lax.ppermute(shard, axis, [(i, (i + by) % length) for i in range(length)])


def tree_sum(value, axis):
    length = lax.axis_size(axis)
    distance = 1
    while distance < length:
        partner = [(i, i ^ distance) for i in range(length)]
        value = value + lax.ppermute(value, axis, partner)
        distance *= 2
    return value


def row_update(cols_ref, blocks, extended, state, row, live, nnz):
    acc = jnp.zeros(state.shape, jnp.float32)
    for k in range(nnz):
        col = cols_ref[row * nnz + k]
        acc = acc + jnp.dot(blocks[k], extended[col], preferred_element_type=jnp.float32)
    return state + jnp.where(live, acc, 0.0)


def load_extended(own_hbm, low_hbm, high_hbm, extended, sems):
    slots = own_hbm.shape[0]
    halo = low_hbm.shape[0]
    copies = [
        pltpu.make_async_copy(own_hbm, extended.at[pl.ds(0, slots)], sems.at[0]),
        pltpu.make_async_copy(low_hbm, extended.at[pl.ds(slots, halo)], sems.at[1]),
        pltpu.make_async_copy(high_hbm, extended.at[pl.ds(slots + halo, halo)], sems.at[2]),
    ]
    for copy in copies:
        copy.start()
    return copies


def send_kernel(cols_ref, count_ref, sends_ref, own_hbm, low_hbm, high_hbm, blocks_hbm, state_hbm,
                to_lower_ref, to_upper_ref, extended, block_buf, state_buf, sems, row_sems, *, nnz):
    rows = block_buf.shape[0]
    copies = load_extended(own_hbm, low_hbm, high_hbm, extended, sems)
    row_copies = []
    for j in range(rows):
        row = sends_ref[j]
        pair = (
            pltpu.make_async_copy(blocks_hbm.at[row], block_buf.at[j], row_sems.at[0, j]),
            pltpu.make_async_copy(state_hbm.at[row], state_buf.at[j], row_sems.at[1, j]),
        )
        for copy in pair:
            copy.start()
        row_copies.append(pair)
    for copy in copies:
        copy.wait()
    count = count_ref[0]
    half = rows // 2
    for j in range(rows):
        for copy in row_copies[j]:
            copy.wait()
        row = sends_ref[j]
        new = row_update(cols_ref, block_buf.at[j], extended, state_buf[j], row, row < count, nnz)
        if j < half:
            to_lower_ref[j] = new.astype(jnp.bfloat16)
        else:
            to_upper_ref[j - half] = new.astype(jnp.bfloat16)


def send_rows(cols, count, sends, rounded, from_lower, from_upper, blocks, state):
    slots, width, vectors = state.shape
    nnz = blocks.shape[1]
    halo = from_lower.shape[0]
    rows = sends.shape[0]
    kernel = functools.partial(send_kernel, nnz=nnz)
    grid_spec = pltpu.PrefetchScalarGridSpec(
        num_scalar_prefetch=3,
        grid=(),
        in_specs=[pl.BlockSpec(memory_space=pl.ANY)] * 5,
        out_specs=[pl.BlockSpec(memory_space=pltpu.VMEM)] * 2,
        scratch_shapes=[
            pltpu.VMEM((slots + 2 * halo, width, vectors), jnp.bfloat16),
            pltpu.VMEM((rows, nnz, width, width), jnp.bfloat16),
            pltpu.VMEM((rows, width, vectors), jnp.float32),
            pltpu.SemaphoreType.DMA((3,)),
            pltpu.SemaphoreType.DMA((2, rows)),
        ],
    )
    return pl.pallas_call(
        kernel,
        grid_spec=grid_spec,
        out_shape=[jax.ShapeDtypeStruct((rows // 2, width, vectors), jnp.bfloat16)] * 2,
    )(cols, count, sends, rounded, from_lower, from_upper, blocks, state)


def substep_kernel(cols_ref, count_ref, own_hbm, low_hbm, high_hbm, blocks_ref, state_ref,
                   new_state_ref, out_ref, extended, sems, *, nnz, per_step, last):
    step = pl.program_id(0)

    @pl.when(step == 0)
    def _():
        for copy in load_extended(own_hbm, low_hbm, high_hbm, extended, sems):
            copy.wait()

    count = count_ref[0]
    for r in range(per_step):
        row = step * per_step + r
        new = row_update(cols_ref, blocks_ref.at[r], extended, state_ref[r], row, row < count, nnz)
        new_state_ref[r] = new
        if not last:
            out_ref[r] = new.astype(jnp.bfloat16)
            continue
        part = lax.dot_general(new, new, (((0,), (0,)), ((), ())), precision=lax.Precision.HIGHEST,
                               preferred_element_type=jnp.float32)
        if r == 0:
            @pl.when(step == 0)
            def _():
                out_ref[...] = jnp.zeros_like(out_ref)
        out_ref[...] += part


def substep(cols, count, rounded, from_lower, from_upper, blocks, state, last):
    slots, width, vectors = state.shape
    nnz = blocks.shape[1]
    halo = from_lower.shape[0]
    per_step = ROWS_PER_STEP
    kernel = functools.partial(substep_kernel, nnz=nnz, per_step=per_step, last=last)
    grid_spec = pltpu.PrefetchScalarGridSpec(
        num_scalar_prefetch=2,
        grid=(slots // per_step,),
        in_specs=[
            pl.BlockSpec(memory_space=pl.ANY),
            pl.BlockSpec(memory_space=pl.ANY),
            pl.BlockSpec(memory_space=pl.ANY),
            pl.BlockSpec((per_step, nnz, width, width), lambda i, c, n: (i, 0, 0, 0)),
            pl.BlockSpec((per_step, width, vectors), lambda i, c, n: (i, 0, 0)),
        ],
        out_specs=[
            pl.BlockSpec((per_step, width, vectors), lambda i, c, n: (i, 0, 0)),
            pl.BlockSpec((vectors, vectors), lambda i, c, n: (0, 0)) if last
            else pl.BlockSpec((per_step, width, vectors), lambda i, c, n: (i, 0, 0)),
        ],
        scratch_shapes=[
            pltpu.VMEM((slots + 2 * halo, width, vectors), jnp.bfloat16),
            pltpu.SemaphoreType.DMA((3,)),
        ],
    )
    return pl.pallas_call(
        kernel,
        grid_spec=grid_spec,
        out_shape=[
            jax.ShapeDtypeStruct(state.shape, jnp.float32),
            jax.ShapeDtypeStruct((vectors, vectors), jnp.float32) if last
            else jax.ShapeDtypeStruct(state.shape, jnp.bfloat16),
        ],
        compiler_params=pltpu.CompilerParams(dimension_semantics=("arbitrary",)),
    )(cols, count, rounded, from_lower, from_upper, blocks, state)


def local(tangent, blocks, columns, counts, send_lists):
    slots, width, vectors = tangent.shape
    live = (jnp.arange(slots, dtype=jnp.int32) < counts[0]).astype(jnp.float32)[:, None, None]
    state = tangent * live
    rounded = state.astype(jnp.bfloat16)
    cols = columns.reshape(-1)
    sends = send_lists.reshape(-1)
    to_lower = rounded[send_lists[0, 0]]
    to_upper = rounded[send_lists[0, 1]]
    for step in range(SUBSTEPS):
        from_lower = passed_along(to_upper, "grains", 1)
        from_upper = passed_along(to_lower, "grains", -1)
        if step < SUBSTEPS - 1:
            to_lower, to_upper = send_rows(cols, counts, sends, rounded, from_lower, from_upper, blocks, state)
        state, rounded = substep(cols, counts, rounded, from_lower, from_upper, blocks, state,
                                 step == SUBSTEPS - 1)
    gram = rounded
    flat = state.reshape(slots * width, vectors)
    first_low = jnp.linalg.cholesky(tree_sum(gram, "grains"))
    inverse = lax.linalg.triangular_solve(
        first_low, jnp.eye(vectors, dtype=jnp.float32), left_side=True, lower=True
    )
    basis = jnp.dot(flat, inverse.T, precision=lax.Precision.HIGHEST)
    r_factor = first_low.T
    return (basis.reshape(slots, width, vectors), r_factor)


def solution(mesh):
    in_specs = (
        P("grains", None, None),
        P("grains", None, None, None),
        P("grains", None),
        P("grains"),
        P("grains", None, None),
    )
    out_specs = (P("grains", None, None), P())
    return jax.shard_map(local, mesh=mesh, in_specs=in_specs, out_specs=out_specs, check_vma=False)
```

```python
import functools

import jax
import jax.numpy as jnp
from jax import lax
from jax.experimental import pallas as pl
from jax.experimental.pallas import tpu as pltpu
from jax.sharding import PartitionSpec as P

SUBSTEPS = 3
ROWS_PER_STEP = 16
SEND_WINDOW = 4


def passed_along(shard, axis, by):
    length = lax.axis_size(axis)
    return lax.ppermute(shard, axis, [(i, (i + by) % length) for i in range(length)])


def tree_sum(value, axis):
    length = lax.axis_size(axis)
    distance = 1
    while distance < length:
        partner = [(i, i ^ distance) for i in range(length)]
        value = value + lax.ppermute(value, axis, partner)
        distance *= 2
    return value


def row_update(cols_ref, blocks, extended, state, row, live, nnz):
    acc = jnp.zeros(state.shape, jnp.float32)
    for k in range(nnz):
        col = cols_ref[row * nnz + k]
        acc = acc + jnp.dot(blocks[k], extended[col], preferred_element_type=jnp.float32)
    return state + jnp.where(live, acc, 0.0)


def load_extended(own_hbm, low_hbm, high_hbm, extended, sems):
    slots = own_hbm.shape[0]
    halo = low_hbm.shape[0]
    copies = [
        pltpu.make_async_copy(own_hbm, extended.at[pl.ds(0, slots)], sems.at[0]),
        pltpu.make_async_copy(low_hbm, extended.at[pl.ds(slots, halo)], sems.at[1]),
        pltpu.make_async_copy(high_hbm, extended.at[pl.ds(slots + halo, halo)], sems.at[2]),
    ]
    for copy in copies:
        copy.start()
    return copies


def send_kernel(cols_ref, count_ref, sends_ref, own_hbm, low_hbm, high_hbm, blocks_hbm, state_hbm,
                to_lower_ref, to_upper_ref, extended, block_buf, state_buf, sems, row_sems, *, nnz, rows):
    window = block_buf.shape[0]
    copies = load_extended(own_hbm, low_hbm, high_hbm, extended, sems)

    def row_copies(j):
        row = sends_ref[j]
        slot = j % window
        return (
            pltpu.make_async_copy(blocks_hbm.at[row], block_buf.at[slot], row_sems.at[0, slot]),
            pltpu.make_async_copy(state_hbm.at[row], state_buf.at[slot], row_sems.at[1, slot]),
        )

    for j in range(min(window, rows)):
        for copy in row_copies(j):
            copy.start()
    for copy in copies:
        copy.wait()
    count = count_ref[0]
    half = rows // 2
    for j in range(rows):
        for copy in row_copies(j):
            copy.wait()
        row = sends_ref[j]
        slot = j % window
        new = row_update(cols_ref, block_buf.at[slot], extended, state_buf[slot], row, row < count, nnz)
        if j < half:
            to_lower_ref[j] = new.astype(jnp.bfloat16)
        else:
            to_upper_ref[j - half] = new.astype(jnp.bfloat16)
        if j + window < rows:
            for copy in row_copies(j + window):
                copy.start()


def send_rows(cols, count, sends, rounded, from_lower, from_upper, blocks, state):
    slots, width, vectors = state.shape
    nnz = blocks.shape[1]
    halo = from_lower.shape[0]
    rows = sends.shape[0]
    window = SEND_WINDOW
    kernel = functools.partial(send_kernel, nnz=nnz, rows=rows)
    grid_spec = pltpu.PrefetchScalarGridSpec(
        num_scalar_prefetch=3,
        grid=(),
        in_specs=[pl.BlockSpec(memory_space=pl.ANY)] * 5,
        out_specs=[pl.BlockSpec(memory_space=pltpu.VMEM)] * 2,
        scratch_shapes=[
            pltpu.VMEM((slots + 2 * halo, width, vectors), jnp.bfloat16),
            pltpu.VMEM((window, nnz, width, width), jnp.bfloat16),
            pltpu.VMEM((window, width, vectors), jnp.float32),
            pltpu.SemaphoreType.DMA((3,)),
            pltpu.SemaphoreType.DMA((2, window)),
        ],
    )
    return pl.pallas_call(
        kernel,
        grid_spec=grid_spec,
        out_shape=[jax.ShapeDtypeStruct((rows // 2, width, vectors), jnp.bfloat16)] * 2,
    )(cols, count, sends, rounded, from_lower, from_upper, blocks, state)


def substep_kernel(cols_ref, count_ref, own_hbm, low_hbm, high_hbm, blocks_ref, state_ref,
                   *rest, nnz, per_step, last, base):
    new_state_ref, out_ref, extended, sems = rest[-4:]
    step = pl.program_id(0)

    @pl.when(step == 0)
    def _():
        for copy in load_extended(own_hbm, low_hbm, high_hbm, extended, sems):
            copy.wait()

    count = count_ref[0]
    for r in range(per_step):
        row = (step + base) * per_step + r
        new = row_update(cols_ref, blocks_ref.at[r], extended, state_ref[r], row, row < count, nnz)
        new_state_ref[r] = new
        if not last:
            out_ref[r] = new.astype(jnp.bfloat16)
            continue
        part = lax.dot_general(new, new, (((0,), (0,)), ((), ())), precision=lax.Precision.HIGHEST,
                               preferred_element_type=jnp.float32)
        if r == 0:
            @pl.when(step == 0)
            def _():
                out_ref[...] = jnp.zeros_like(out_ref)
        out_ref[...] += part


def substep(cols, count, rounded, from_lower, from_upper, blocks, state, last, part=0, parts=1, prev=()):
    slots, width, vectors = state.shape
    nnz = blocks.shape[1]
    halo = from_lower.shape[0]
    per_step = ROWS_PER_STEP
    steps = slots // per_step // parts
    base = part * steps
    kernel = functools.partial(substep_kernel, nnz=nnz, per_step=per_step, last=last, base=base)
    grid_spec = pltpu.PrefetchScalarGridSpec(
        num_scalar_prefetch=2,
        grid=(steps,),
        in_specs=[
            pl.BlockSpec(memory_space=pl.ANY),
            pl.BlockSpec(memory_space=pl.ANY),
            pl.BlockSpec(memory_space=pl.ANY),
            pl.BlockSpec((per_step, nnz, width, width), lambda i, c, n: (i + base, 0, 0, 0)),
            pl.BlockSpec((per_step, width, vectors), lambda i, c, n: (i + base, 0, 0)),
        ] + [pl.BlockSpec(memory_space=pl.ANY)] * len(prev),
        out_specs=[
            pl.BlockSpec((per_step, width, vectors), lambda i, c, n: (i + base, 0, 0)),
            pl.BlockSpec((vectors, vectors), lambda i, c, n: (0, 0)) if last
            else pl.BlockSpec((per_step, width, vectors), lambda i, c, n: (i + base, 0, 0)),
        ],
        scratch_shapes=[
            pltpu.VMEM((slots + 2 * halo, width, vectors), jnp.bfloat16),
            pltpu.SemaphoreType.DMA((3,)),
        ],
    )
    return pl.pallas_call(
        kernel,
        grid_spec=grid_spec,
        out_shape=[
            jax.ShapeDtypeStruct(state.shape, jnp.float32),
            jax.ShapeDtypeStruct((vectors, vectors), jnp.float32) if last
            else jax.ShapeDtypeStruct(state.shape, jnp.bfloat16),
        ],
        input_output_aliases={7 + i: i for i in range(len(prev))},
        compiler_params=pltpu.CompilerParams(dimension_semantics=("arbitrary",)),
    )(cols, count, rounded, from_lower, from_upper, blocks, state, *prev)


def local(tangent, blocks, columns, counts, send_lists):
    slots, width, vectors = tangent.shape
    live = (jnp.arange(slots, dtype=jnp.int32) < counts[0]).astype(jnp.float32)[:, None, None]
    state = tangent * live
    rounded = state.astype(jnp.bfloat16)
    cols = columns.reshape(-1)
    sends = send_lists.reshape(-1)
    to_lower = rounded[send_lists[0, 0]]
    to_upper = rounded[send_lists[0, 1]]
    from_lower = passed_along(to_upper, "grains", 1)
    from_upper = passed_along(to_lower, "grains", -1)
    for step in range(SUBSTEPS - 1):
        to_lower, to_upper = send_rows(cols, counts, sends, rounded, from_lower, from_upper, blocks, state)
        next_upper = passed_along(to_lower, "grains", -1)
        first = substep(cols, counts, rounded, from_lower, from_upper, blocks, state, False, 0, 2)
        to_upper, first = lax.optimization_barrier((to_upper, first))
        next_lower = passed_along(to_upper, "grains", 1)
        state, rounded = substep(cols, counts, rounded, from_lower, from_upper, blocks, state, False, 1, 2, first)
        from_lower, from_upper = next_lower, next_upper
    state, rounded = substep(cols, counts, rounded, from_lower, from_upper, blocks, state, True)
    gram = rounded
    flat = state.reshape(slots * width, vectors)
    first_low = jnp.linalg.cholesky(tree_sum(gram, "grains"))
    inverse = lax.linalg.triangular_solve(
        first_low, jnp.eye(vectors, dtype=jnp.float32), left_side=True, lower=True
    )
    basis = jnp.dot(flat, inverse.T, precision=lax.Precision.HIGHEST)
    r_factor = first_low.T
    return (basis.reshape(slots, width, vectors), r_factor)


def solution(mesh):
    in_specs = (
        P("grains", None, None),
        P("grains", None, None, None),
        P("grains", None),
        P("grains"),
        P("grains", None, None),
    )
    out_specs = (P("grains", None, None), P())
    return jax.shard_map(local, mesh=mesh, in_specs=in_specs, out_specs=out_specs, check_vma=False)
```

```python
import functools

import jax
import jax.numpy as jnp
from jax import lax
from jax.experimental import pallas as pl
from jax.experimental.pallas import tpu as pltpu
from jax.sharding import PartitionSpec as P

SUBSTEPS = 3
ROWS_PER_STEP = 16


def passed_along(shard, axis, by):
    length = lax.axis_size(axis)
    return lax.ppermute(shard, axis, [(i, (i + by) % length) for i in range(length)])


def tree_sum(value, axis):
    length = lax.axis_size(axis)
    masks = [1]
    bit = 2
    while bit < length:
        masks += [bit, 3 * bit] if 4 * bit <= length else [bit]
        bit *= 4
    for mask in masks:
        partner = [(i, i ^ mask) for i in range(length)]
        value = value + lax.ppermute(value, axis, partner)
    return value


def substep_kernel(cols_ref, count_ref, sends_ref, own_hbm, low_hbm, high_hbm, blocks_ref, state_ref,
                   new_state_ref, out_ref, *rest, nnz, per_step, last):
    if last:
        extended, sems = rest
    else:
        to_lower_ref, to_upper_ref, extended, sems = rest
    step = pl.program_id(0)
    slots = own_hbm.shape[0]
    halo = low_hbm.shape[0]

    @pl.when(step == 0)
    def _():
        copies = [
            pltpu.make_async_copy(own_hbm, extended.at[pl.ds(0, slots)], sems.at[0]),
            pltpu.make_async_copy(low_hbm, extended.at[pl.ds(slots, halo)], sems.at[1]),
            pltpu.make_async_copy(high_hbm, extended.at[pl.ds(slots + halo, halo)], sems.at[2]),
        ]
        for copy in copies:
            copy.start()
        for copy in copies:
            copy.wait()

    count = count_ref[0]
    for r in range(per_step):
        row = step * per_step + r
        acc = jnp.zeros(state_ref.shape[1:], jnp.float32)
        for k in range(nnz):
            col = cols_ref[row * nnz + k]
            acc = acc + jnp.dot(blocks_ref[r, k], extended[col], preferred_element_type=jnp.float32)
        new = state_ref[r] + jnp.where(row < count, acc, 0.0)
        new_state_ref[r] = new
        if not last:
            out_ref[r] = new.astype(jnp.bfloat16)
            continue
        part = lax.dot_general(new, new, (((0,), (0,)), ((), ())), precision=lax.Precision.HIGHEST,
                               preferred_element_type=jnp.float32)
        if r == 0:
            @pl.when(step == 0)
            def _():
                out_ref[...] = jnp.zeros_like(out_ref)
        out_ref[...] += part
    if last:
        return
    half = to_lower_ref.shape[0]
    for j in range(2 * half):
        local = sends_ref[j] - step * per_step

        @pl.when((local >= 0) & (local < per_step))
        def _():
            if j < half:
                to_lower_ref[j] = out_ref[local]
            else:
                to_upper_ref[j - half] = out_ref[local]


def substep(cols, count, sends, rounded, from_lower, from_upper, blocks, state, last):
    slots, width, vectors = state.shape
    nnz = blocks.shape[1]
    halo = from_lower.shape[0]
    per_step = ROWS_PER_STEP
    kernel = functools.partial(substep_kernel, nnz=nnz, per_step=per_step, last=last)
    grid_spec = pltpu.PrefetchScalarGridSpec(
        num_scalar_prefetch=3,
        grid=(slots // per_step,),
        in_specs=[
            pl.BlockSpec(memory_space=pl.ANY),
            pl.BlockSpec(memory_space=pl.ANY),
            pl.BlockSpec(memory_space=pl.ANY),
            pl.BlockSpec((per_step, nnz, width, width), lambda i, c, n, q: (i, 0, 0, 0)),
            pl.BlockSpec((per_step, width, vectors), lambda i, c, n, q: (i, 0, 0)),
        ],
        out_specs=[
            pl.BlockSpec((per_step, width, vectors), lambda i, c, n, q: (i, 0, 0)),
            pl.BlockSpec((vectors, vectors), lambda i, c, n, q: (0, 0)) if last
            else pl.BlockSpec((per_step, width, vectors), lambda i, c, n, q: (i, 0, 0)),
        ] + ([] if last else [pl.BlockSpec((halo, width, vectors), lambda i, c, n, q: (0, 0, 0))] * 2),
        scratch_shapes=[
            pltpu.VMEM((slots + 2 * halo, width, vectors), jnp.bfloat16),
            pltpu.SemaphoreType.DMA((3,)),
        ],
    )
    return pl.pallas_call(
        kernel,
        grid_spec=grid_spec,
        out_shape=[
            jax.ShapeDtypeStruct(state.shape, jnp.float32),
            jax.ShapeDtypeStruct((vectors, vectors), jnp.float32) if last
            else jax.ShapeDtypeStruct(state.shape, jnp.bfloat16),
        ] + ([] if last else [jax.ShapeDtypeStruct((halo, width, vectors), jnp.bfloat16)] * 2),
        compiler_params=pltpu.CompilerParams(dimension_semantics=("arbitrary",)),
    )(cols, count, sends, rounded, from_lower, from_upper, blocks, state)


def local(tangent, blocks, columns, counts, send_lists):
    slots, width, vectors = tangent.shape
    live = (jnp.arange(slots, dtype=jnp.int32) < counts[0]).astype(jnp.float32)[:, None, None]
    state = tangent * live
    rounded = state.astype(jnp.bfloat16)
    cols = columns.reshape(-1)
    sends = send_lists.reshape(-1)
    to_lower = tangent[send_lists[0, 0]].astype(jnp.bfloat16)
    to_upper = tangent[send_lists[0, 1]].astype(jnp.bfloat16)
    for step in range(SUBSTEPS):
        from_lower = passed_along(to_upper, "grains", 1)
        from_upper = passed_along(to_lower, "grains", -1)
        if step < SUBSTEPS - 1:
            state, rounded, to_lower, to_upper = substep(
                cols, counts, sends, rounded, from_lower, from_upper, blocks, state, False)
        else:
            state, gram = substep(cols, counts, sends, rounded, from_lower, from_upper, blocks, state, True)
    flat = state.reshape(slots * width, vectors)
    first_low = jnp.linalg.cholesky(tree_sum(gram, "grains"))
    inverse = lax.linalg.triangular_solve(
        first_low, jnp.eye(vectors, dtype=jnp.float32), left_side=True, lower=True
    )
    basis = jnp.dot(flat, inverse.T, precision=lax.Precision.HIGHEST)
    r_factor = first_low.T
    return (basis.reshape(slots, width, vectors), r_factor)


def solution(mesh):
    in_specs = (
        P("grains", None, None),
        P("grains", None, None, None),
        P("grains", None),
        P("grains"),
        P("grains", None, None),
    )
    out_specs = (P("grains", None, None), P())
    return jax.shard_map(local, mesh=mesh, in_specs=in_specs, out_specs=out_specs, check_vma=False)
```

```python
import functools

import jax
import jax.numpy as jnp
from jax import lax
from jax.experimental import pallas as pl
from jax.experimental.pallas import tpu as pltpu
from jax.sharding import PartitionSpec as P

SUBSTEPS = 3
ROWS_PER_STEP = 16


def passed_along(shard, axis, by):
    length = lax.axis_size(axis)
    return lax.ppermute(shard, axis, [(i, (i + by) % length) for i in range(length)])


def tree_sum(value, axis):
    length = lax.axis_size(axis)
    masks = [1]
    bit = 2
    while bit < length:
        masks += [bit, 3 * bit] if 4 * bit <= length else [bit]
        bit *= 4
    for mask in masks:
        partner = [(i, i ^ mask) for i in range(length)]
        value = value + lax.ppermute(value, axis, partner)
    return value


def pick_kernel(sends_ref, tangent_hbm, to_lower_ref, to_upper_ref, buf, sems):
    rows = buf.shape[0]
    half = rows // 2
    copies = [pltpu.make_async_copy(tangent_hbm.at[sends_ref[j]], buf.at[j], sems.at[j]) for j in range(rows)]
    for copy in copies:
        copy.start()
    for j in range(rows):
        copies[j].wait()
        if j < half:
            to_lower_ref[j] = buf[j].astype(jnp.bfloat16)
        else:
            to_upper_ref[j - half] = buf[j].astype(jnp.bfloat16)


def pick_rows(sends, tangent):
    rows = sends.shape[0]
    slots, width, vectors = tangent.shape
    grid_spec = pltpu.PrefetchScalarGridSpec(
        num_scalar_prefetch=1,
        grid=(),
        in_specs=[pl.BlockSpec(memory_space=pl.ANY)],
        out_specs=[pl.BlockSpec(memory_space=pltpu.VMEM)] * 2,
        scratch_shapes=[pltpu.VMEM((rows, width, vectors), jnp.float32), pltpu.SemaphoreType.DMA((rows,))],
    )
    return pl.pallas_call(
        pick_kernel,
        grid_spec=grid_spec,
        out_shape=[jax.ShapeDtypeStruct((rows // 2, width, vectors), jnp.bfloat16)] * 2,
    )(sends, tangent)


def substep_kernel(cols_ref, count_ref, sends_ref, own_hbm, low_hbm, high_hbm, blocks_ref, state_ref,
                   new_state_ref, out_ref, *rest, nnz, per_step, last):
    if last:
        extended, sems = rest
    else:
        to_lower_ref, to_upper_ref, extended, sems = rest
    step = pl.program_id(0)
    slots = own_hbm.shape[0]
    halo = low_hbm.shape[0]

    @pl.when(step == 0)
    def _():
        copies = [
            pltpu.make_async_copy(own_hbm, extended.at[pl.ds(0, slots)], sems.at[0]),
            pltpu.make_async_copy(low_hbm, extended.at[pl.ds(slots, halo)], sems.at[1]),
            pltpu.make_async_copy(high_hbm, extended.at[pl.ds(slots + halo, halo)], sems.at[2]),
        ]
        for copy in copies:
            copy.start()
        for copy in copies:
            copy.wait()

    count = count_ref[0]
    for r in range(per_step):
        row = step * per_step + r
        acc = jnp.zeros(state_ref.shape[1:], jnp.float32)
        for k in range(nnz):
            col = cols_ref[row * nnz + k]
            acc = acc + jnp.dot(blocks_ref[r, k], extended[col], preferred_element_type=jnp.float32)
        new = state_ref[r] + jnp.where(row < count, acc, 0.0)
        new_state_ref[r] = new
        if not last:
            out_ref[r] = new.astype(jnp.bfloat16)
            continue
        part = lax.dot_general(new, new, (((0,), (0,)), ((), ())), precision=lax.Precision.HIGHEST,
                               preferred_element_type=jnp.float32)
        if r == 0:
            @pl.when(step == 0)
            def _():
                out_ref[...] = jnp.zeros_like(out_ref)
        out_ref[...] += part
    if last:
        return
    half = to_lower_ref.shape[0]
    for j in range(2 * half):
        local = sends_ref[j] - step * per_step

        @pl.when((local >= 0) & (local < per_step))
        def _():
            if j < half:
                to_lower_ref[j] = out_ref[local]
            else:
                to_upper_ref[j - half] = out_ref[local]


def substep(cols, count, sends, rounded, from_lower, from_upper, blocks, state, last):
    slots, width, vectors = state.shape
    nnz = blocks.shape[1]
    halo = from_lower.shape[0]
    per_step = ROWS_PER_STEP
    kernel = functools.partial(substep_kernel, nnz=nnz, per_step=per_step, last=last)
    grid_spec = pltpu.PrefetchScalarGridSpec(
        num_scalar_prefetch=3,
        grid=(slots // per_step,),
        in_specs=[
            pl.BlockSpec(memory_space=pl.ANY),
            pl.BlockSpec(memory_space=pl.ANY),
            pl.BlockSpec(memory_space=pl.ANY),
            pl.BlockSpec((per_step, nnz, width, width), lambda i, c, n, q: (i, 0, 0, 0)),
            pl.BlockSpec((per_step, width, vectors), lambda i, c, n, q: (i, 0, 0)),
        ],
        out_specs=[
            pl.BlockSpec((per_step, width, vectors), lambda i, c, n, q: (i, 0, 0)),
            pl.BlockSpec((vectors, vectors), lambda i, c, n, q: (0, 0)) if last
            else pl.BlockSpec((per_step, width, vectors), lambda i, c, n, q: (i, 0, 0)),
        ] + ([] if last else [pl.BlockSpec((halo, width, vectors), lambda i, c, n, q: (0, 0, 0))] * 2),
        scratch_shapes=[
            pltpu.VMEM((slots + 2 * halo, width, vectors), jnp.bfloat16),
            pltpu.SemaphoreType.DMA((3,)),
        ],
    )
    return pl.pallas_call(
        kernel,
        grid_spec=grid_spec,
        out_shape=[
            jax.ShapeDtypeStruct(state.shape, jnp.float32),
            jax.ShapeDtypeStruct((vectors, vectors), jnp.float32) if last
            else jax.ShapeDtypeStruct(state.shape, jnp.bfloat16),
        ] + ([] if last else [jax.ShapeDtypeStruct((halo, width, vectors), jnp.bfloat16)] * 2),
        compiler_params=pltpu.CompilerParams(dimension_semantics=("arbitrary",)),
    )(cols, count, sends, rounded, from_lower, from_upper, blocks, state)


def local(tangent, blocks, columns, counts, send_lists):
    slots, width, vectors = tangent.shape
    live = (jnp.arange(slots, dtype=jnp.int32) < counts[0]).astype(jnp.float32)[:, None, None]
    state = tangent * live
    rounded = state.astype(jnp.bfloat16)
    cols = columns.reshape(-1)
    sends = send_lists.reshape(-1)
    to_lower, to_upper = pick_rows(sends, tangent)
    for step in range(SUBSTEPS):
        from_lower = passed_along(to_upper, "grains", 1)
        from_upper = passed_along(to_lower, "grains", -1)
        if step < SUBSTEPS - 1:
            state, rounded, to_lower, to_upper = substep(
                cols, counts, sends, rounded, from_lower, from_upper, blocks, state, False)
        else:
            state, gram = substep(cols, counts, sends, rounded, from_lower, from_upper, blocks, state, True)
    flat = state.reshape(slots * width, vectors)
    first_low = jnp.linalg.cholesky(tree_sum(gram, "grains"))
    inverse = lax.linalg.triangular_solve(
        first_low, jnp.eye(vectors, dtype=jnp.float32), left_side=True, lower=True
    )
    basis = jnp.dot(flat, inverse.T, precision=lax.Precision.HIGHEST)
    r_factor = first_low.T
    return (basis.reshape(slots, width, vectors), r_factor)


def solution(mesh):
    in_specs = (
        P("grains", None, None),
        P("grains", None, None, None),
        P("grains", None),
        P("grains"),
        P("grains", None, None),
    )
    out_specs = (P("grains", None, None), P())
    return jax.shard_map(local, mesh=mesh, in_specs=in_specs, out_specs=out_specs, check_vma=False)
```

```python
import functools

import jax
import jax.numpy as jnp
from jax import lax
from jax.experimental import pallas as pl
from jax.experimental.pallas import tpu as pltpu
from jax.sharding import PartitionSpec as P

SUBSTEPS = 3
ROWS_PER_STEP = 16


def passed_along(shard, axis, by):
    length = lax.axis_size(axis)
    return lax.ppermute(shard, axis, [(i, (i + by) % length) for i in range(length)])


def tree_sum(value, axis):
    length = lax.axis_size(axis)
    masks = [1]
    bit = 2
    while bit < length:
        masks += [bit, 3 * bit] if 4 * bit <= length else [bit]
        bit *= 4
    for mask in masks:
        partner = [(i, i ^ mask) for i in range(length)]
        value = value + lax.ppermute(value, axis, partner)
    return value


def pick_kernel(sends_ref, tangent_hbm, to_lower_ref, to_upper_ref, buf, sems):
    rows = buf.shape[0]
    half = rows // 2
    copies = [pltpu.make_async_copy(tangent_hbm.at[sends_ref[0, j // half, j % half]], buf.at[j], sems.at[j])
              for j in range(rows)]
    for copy in copies:
        copy.start()
    for j in range(rows):
        copies[j].wait()
        if j < half:
            to_lower_ref[j] = buf[j].astype(jnp.bfloat16)
        else:
            to_upper_ref[j - half] = buf[j].astype(jnp.bfloat16)


def pick_rows(sends, tangent):
    rows = sends.shape[1] * sends.shape[2]
    slots, width, vectors = tangent.shape
    grid_spec = pltpu.PrefetchScalarGridSpec(
        num_scalar_prefetch=1,
        grid=(),
        in_specs=[pl.BlockSpec(memory_space=pl.ANY)],
        out_specs=[pl.BlockSpec(memory_space=pltpu.VMEM)] * 2,
        scratch_shapes=[pltpu.VMEM((rows, width, vectors), jnp.float32), pltpu.SemaphoreType.DMA((rows,))],
    )
    return pl.pallas_call(
        pick_kernel,
        grid_spec=grid_spec,
        out_shape=[jax.ShapeDtypeStruct((rows // 2, width, vectors), jnp.bfloat16)] * 2,
    )(sends, tangent)


def substep_kernel(cols_ref, count_ref, sends_ref, own_hbm, low_hbm, high_hbm, blocks_ref, state_ref,
                   new_state_ref, out_ref, *rest, nnz, per_step, last):
    if last:
        extended, sems = rest
    else:
        to_lower_ref, to_upper_ref, extended, sems = rest
    step = pl.program_id(0)
    slots = own_hbm.shape[0]
    halo = low_hbm.shape[0]

    @pl.when(step == 0)
    def _():
        copies = [
            pltpu.make_async_copy(own_hbm, extended.at[pl.ds(0, slots)], sems.at[0]),
            pltpu.make_async_copy(low_hbm, extended.at[pl.ds(slots, halo)], sems.at[1]),
            pltpu.make_async_copy(high_hbm, extended.at[pl.ds(slots + halo, halo)], sems.at[2]),
        ]
        for copy in copies:
            copy.start()
        for copy in copies:
            copy.wait()

    count = count_ref[0]
    for r in range(per_step):
        row = step * per_step + r
        acc = jnp.zeros(state_ref.shape[1:], jnp.float32)
        for k in range(nnz):
            col = cols_ref[row, k]
            acc = acc + jnp.dot(blocks_ref[r, k], extended[col], preferred_element_type=jnp.float32)
        new = state_ref[r] + jnp.where(row < count, acc, 0.0)
        new_state_ref[r] = new
        if not last:
            out_ref[r] = new.astype(jnp.bfloat16)
            continue
        part = lax.dot_general(new, new, (((0,), (0,)), ((), ())), precision=lax.Precision.HIGHEST,
                               preferred_element_type=jnp.float32)
        if r == 0:
            @pl.when(step == 0)
            def _():
                out_ref[...] = jnp.zeros_like(out_ref)
        out_ref[...] += part
    if last:
        return
    half = to_lower_ref.shape[0]
    for j in range(2 * half):
        local = sends_ref[0, j // half, j % half] - step * per_step

        @pl.when((local >= 0) & (local < per_step))
        def _():
            if j < half:
                to_lower_ref[j] = out_ref[local]
            else:
                to_upper_ref[j - half] = out_ref[local]


def substep(cols, count, sends, rounded, from_lower, from_upper, blocks, state, last):
    slots, width, vectors = state.shape
    nnz = blocks.shape[1]
    halo = from_lower.shape[0]
    per_step = ROWS_PER_STEP
    kernel = functools.partial(substep_kernel, nnz=nnz, per_step=per_step, last=last)
    grid_spec = pltpu.PrefetchScalarGridSpec(
        num_scalar_prefetch=3,
        grid=(slots // per_step,),
        in_specs=[
            pl.BlockSpec(memory_space=pl.ANY),
            pl.BlockSpec(memory_space=pl.ANY),
            pl.BlockSpec(memory_space=pl.ANY),
            pl.BlockSpec((per_step, nnz, width, width), lambda i, c, n, q: (i, 0, 0, 0)),
            pl.BlockSpec((per_step, width, vectors), lambda i, c, n, q: (i, 0, 0)),
        ],
        out_specs=[
            pl.BlockSpec((per_step, width, vectors), lambda i, c, n, q: (i, 0, 0)),
            pl.BlockSpec((vectors, vectors), lambda i, c, n, q: (0, 0)) if last
            else pl.BlockSpec((per_step, width, vectors), lambda i, c, n, q: (i, 0, 0)),
        ] + ([] if last else [pl.BlockSpec((halo, width, vectors), lambda i, c, n, q: (0, 0, 0))] * 2),
        scratch_shapes=[
            pltpu.VMEM((slots + 2 * halo, width, vectors), jnp.bfloat16),
            pltpu.SemaphoreType.DMA((3,)),
        ],
    )
    return pl.pallas_call(
        kernel,
        grid_spec=grid_spec,
        out_shape=[
            jax.ShapeDtypeStruct(state.shape, jnp.float32),
            jax.ShapeDtypeStruct((vectors, vectors), jnp.float32) if last
            else jax.ShapeDtypeStruct(state.shape, jnp.bfloat16),
        ] + ([] if last else [jax.ShapeDtypeStruct((halo, width, vectors), jnp.bfloat16)] * 2),
        compiler_params=pltpu.CompilerParams(dimension_semantics=("arbitrary",)),
    )(cols, count, sends, rounded, from_lower, from_upper, blocks, state)


def local(tangent, blocks, columns, counts, send_lists):
    slots, width, vectors = tangent.shape
    live = (jnp.arange(slots, dtype=jnp.int32) < counts[0]).astype(jnp.float32)[:, None, None]
    state = tangent * live
    rounded = state.astype(jnp.bfloat16)
    cols = columns
    sends = send_lists
    to_lower, to_upper = pick_rows(sends, tangent)
    for step in range(SUBSTEPS):
        from_lower = passed_along(to_upper, "grains", 1)
        from_upper = passed_along(to_lower, "grains", -1)
        if step < SUBSTEPS - 1:
            state, rounded, to_lower, to_upper = substep(
                cols, counts, sends, rounded, from_lower, from_upper, blocks, state, False)
        else:
            state, gram = substep(cols, counts, sends, rounded, from_lower, from_upper, blocks, state, True)
    flat = state.reshape(slots * width, vectors)
    first_low = jnp.linalg.cholesky(tree_sum(gram, "grains"))
    inverse = lax.linalg.triangular_solve(
        first_low, jnp.eye(vectors, dtype=jnp.float32), left_side=True, lower=True
    )
    basis = jnp.dot(flat, inverse.T, precision=lax.Precision.HIGHEST)
    r_factor = first_low.T
    return (basis.reshape(slots, width, vectors), r_factor)


def solution(mesh):
    in_specs = (
        P("grains", None, None),
        P("grains", None, None, None),
        P("grains", None),
        P("grains"),
        P("grains", None, None),
    )
    out_specs = (P("grains", None, None), P())
    return jax.shard_map(local, mesh=mesh, in_specs=in_specs, out_specs=out_specs, check_vma=False)
```

```python
import functools

import jax
import jax.numpy as jnp
from jax import lax
from jax.experimental import pallas as pl
from jax.experimental.pallas import tpu as pltpu
from jax.sharding import PartitionSpec as P

SUBSTEPS = 3
ROWS_PER_STEP = 16


def passed_along(shard, axis, by):
    length = lax.axis_size(axis)
    return lax.ppermute(shard, axis, [(i, (i + by) % length) for i in range(length)])


def tree_sum(value, axis):
    length = lax.axis_size(axis)
    masks = [1]
    bit = 2
    while bit < length:
        masks += [bit, 3 * bit] if 4 * bit <= length else [bit]
        bit *= 4
    for mask in masks:
        partner = [(i, i ^ mask) for i in range(length)]
        value = value + lax.ppermute(value, axis, partner)
    return value


def pick_kernel(sends_ref, tangent_hbm, to_lower_ref, to_upper_ref, buf, sems):
    rows = buf.shape[0]
    half = rows // 2
    copies = [pltpu.make_async_copy(tangent_hbm.at[sends_ref[j]], buf.at[j], sems.at[j]) for j in range(rows)]
    for copy in copies:
        copy.start()
    for j in range(rows):
        copies[j].wait()
        if j < half:
            to_lower_ref[j] = buf[j].astype(jnp.bfloat16)
        else:
            to_upper_ref[j - half] = buf[j].astype(jnp.bfloat16)


def pick_rows(sends, tangent):
    rows = sends.shape[0]
    slots, width, vectors = tangent.shape
    grid_spec = pltpu.PrefetchScalarGridSpec(
        num_scalar_prefetch=1,
        grid=(),
        in_specs=[pl.BlockSpec(memory_space=pl.ANY)],
        out_specs=[pl.BlockSpec(memory_space=pltpu.VMEM)] * 2,
        scratch_shapes=[pltpu.VMEM((rows, width, vectors), jnp.float32), pltpu.SemaphoreType.DMA((rows,))],
    )
    return pl.pallas_call(
        pick_kernel,
        grid_spec=grid_spec,
        out_shape=[jax.ShapeDtypeStruct((rows // 2, width, vectors), jnp.bfloat16)] * 2,
    )(sends, tangent)


def substep_kernel(cols_ref, count_ref, sends_ref, own_hbm, low_hbm, high_hbm, blocks_ref, state_ref,
                   new_state_ref, out_ref, *rest, nnz, per_step, last):
    if last:
        extended, sems = rest
    else:
        to_lower_ref, to_upper_ref, extended, sems = rest
    step = pl.program_id(0)
    slots = own_hbm.shape[0]
    halo = low_hbm.shape[0]

    @pl.when(step == 0)
    def _():
        copies = [
            pltpu.make_async_copy(own_hbm, extended.at[pl.ds(0, slots)], sems.at[0]),
            pltpu.make_async_copy(low_hbm, extended.at[pl.ds(slots, halo)], sems.at[1]),
            pltpu.make_async_copy(high_hbm, extended.at[pl.ds(slots + halo, halo)], sems.at[2]),
        ]
        for copy in copies:
            copy.start()
        for copy in copies:
            copy.wait()

    count = count_ref[0]
    for r in range(per_step):
        row = step * per_step + r
        acc = jnp.zeros(state_ref.shape[1:], jnp.float32)
        for k in range(nnz):
            col = cols_ref[row * nnz + k]
            acc = acc + jnp.dot(blocks_ref[r, k], extended[col], preferred_element_type=jnp.float32)
        new = state_ref[r] + jnp.where(row < count, acc, 0.0)
        new_state_ref[r] = new
        if not last:
            out_ref[r] = new.astype(jnp.bfloat16)
            continue
        part = lax.dot_general(new, new, (((0,), (0,)), ((), ())), precision=lax.Precision.HIGH,
                               preferred_element_type=jnp.float32)
        if r == 0:
            @pl.when(step == 0)
            def _():
                out_ref[...] = jnp.zeros_like(out_ref)
        out_ref[...] += part
    if last:
        return
    half = to_lower_ref.shape[0]
    for j in range(2 * half):
        local = sends_ref[j] - step * per_step

        @pl.when((local >= 0) & (local < per_step))
        def _():
            if j < half:
                to_lower_ref[j] = out_ref[local]
            else:
                to_upper_ref[j - half] = out_ref[local]


def substep(cols, count, sends, rounded, from_lower, from_upper, blocks, state, last):
    slots, width, vectors = state.shape
    nnz = blocks.shape[1]
    halo = from_lower.shape[0]
    per_step = ROWS_PER_STEP
    kernel = functools.partial(substep_kernel, nnz=nnz, per_step=per_step, last=last)
    grid_spec = pltpu.PrefetchScalarGridSpec(
        num_scalar_prefetch=3,
        grid=(slots // per_step,),
        in_specs=[
            pl.BlockSpec(memory_space=pl.ANY),
            pl.BlockSpec(memory_space=pl.ANY),
            pl.BlockSpec(memory_space=pl.ANY),
            pl.BlockSpec((per_step, nnz, width, width), lambda i, c, n, q: (i, 0, 0, 0)),
            pl.BlockSpec((per_step, width, vectors), lambda i, c, n, q: (i, 0, 0)),
        ],
        out_specs=[
            pl.BlockSpec((per_step, width, vectors), lambda i, c, n, q: (i, 0, 0)),
            pl.BlockSpec((vectors, vectors), lambda i, c, n, q: (0, 0)) if last
            else pl.BlockSpec((per_step, width, vectors), lambda i, c, n, q: (i, 0, 0)),
        ] + ([] if last else [pl.BlockSpec((halo, width, vectors), lambda i, c, n, q: (0, 0, 0))] * 2),
        scratch_shapes=[
            pltpu.VMEM((slots + 2 * halo, width, vectors), jnp.bfloat16),
            pltpu.SemaphoreType.DMA((3,)),
        ],
    )
    return pl.pallas_call(
        kernel,
        grid_spec=grid_spec,
        out_shape=[
            jax.ShapeDtypeStruct(state.shape, jnp.float32),
            jax.ShapeDtypeStruct((vectors, vectors), jnp.float32) if last
            else jax.ShapeDtypeStruct(state.shape, jnp.bfloat16),
        ] + ([] if last else [jax.ShapeDtypeStruct((halo, width, vectors), jnp.bfloat16)] * 2),
        compiler_params=pltpu.CompilerParams(dimension_semantics=("arbitrary",)),
    )(cols, count, sends, rounded, from_lower, from_upper, blocks, state)


def local(tangent, blocks, columns, counts, send_lists):
    slots, width, vectors = tangent.shape
    live = (jnp.arange(slots, dtype=jnp.int32) < counts[0]).astype(jnp.float32)[:, None, None]
    state = tangent * live
    rounded = state.astype(jnp.bfloat16)
    cols = columns.reshape(-1)
    sends = send_lists.reshape(-1)
    to_lower, to_upper = pick_rows(sends, tangent)
    for step in range(SUBSTEPS):
        from_lower = passed_along(to_upper, "grains", 1)
        from_upper = passed_along(to_lower, "grains", -1)
        if step < SUBSTEPS - 1:
            state, rounded, to_lower, to_upper = substep(
                cols, counts, sends, rounded, from_lower, from_upper, blocks, state, False)
        else:
            state, gram = substep(cols, counts, sends, rounded, from_lower, from_upper, blocks, state, True)
    flat = state.reshape(slots * width, vectors)
    first_low = jnp.linalg.cholesky(tree_sum(gram, "grains"))
    inverse = lax.linalg.triangular_solve(
        first_low, jnp.eye(vectors, dtype=jnp.float32), left_side=True, lower=True
    )
    basis = jnp.dot(flat, inverse.T, precision=lax.Precision.HIGH)
    r_factor = first_low.T
    return (basis.reshape(slots, width, vectors), r_factor)


def solution(mesh):
    in_specs = (
        P("grains", None, None),
        P("grains", None, None, None),
        P("grains", None),
        P("grains"),
        P("grains", None, None),
    )
    out_specs = (P("grains", None, None), P())
    return jax.shard_map(local, mesh=mesh, in_specs=in_specs, out_specs=out_specs, check_vma=False)
```

```python
import functools

import jax
import jax.numpy as jnp
from jax import lax
from jax.experimental import pallas as pl
from jax.experimental.pallas import tpu as pltpu
from jax.sharding import PartitionSpec as P

SUBSTEPS = 3
ROWS_PER_STEP = 16


def passed_along(shard, axis, by):
    length = lax.axis_size(axis)
    return lax.ppermute(shard, axis, [(i, (i + by) % length) for i in range(length)])


def tree_sum(value, axis):
    length = lax.axis_size(axis)
    masks = [1]
    bit = 2
    while bit < length:
        masks += [bit, 3 * bit] if 4 * bit <= length else [bit]
        bit *= 4
    halves = jnp.split(value, 2, axis=0)
    for mask in masks:
        partner = [(i, i ^ mask) for i in range(length)]
        halves = [half + lax.ppermute(half, axis, partner) for half in halves]
    return jnp.concatenate(halves, axis=0)


def pick_kernel(sends_ref, tangent_hbm, to_lower_ref, to_upper_ref, buf, sems):
    rows = buf.shape[0]
    half = rows // 2
    copies = [pltpu.make_async_copy(tangent_hbm.at[sends_ref[j]], buf.at[j], sems.at[j]) for j in range(rows)]
    for copy in copies:
        copy.start()
    for j in range(rows):
        copies[j].wait()
        if j < half:
            to_lower_ref[j] = buf[j].astype(jnp.bfloat16)
        else:
            to_upper_ref[j - half] = buf[j].astype(jnp.bfloat16)


def pick_rows(sends, tangent):
    rows = sends.shape[0]
    slots, width, vectors = tangent.shape
    grid_spec = pltpu.PrefetchScalarGridSpec(
        num_scalar_prefetch=1,
        grid=(),
        in_specs=[pl.BlockSpec(memory_space=pl.ANY)],
        out_specs=[pl.BlockSpec(memory_space=pltpu.VMEM)] * 2,
        scratch_shapes=[pltpu.VMEM((rows, width, vectors), jnp.float32), pltpu.SemaphoreType.DMA((rows,))],
    )
    return pl.pallas_call(
        pick_kernel,
        grid_spec=grid_spec,
        out_shape=[jax.ShapeDtypeStruct((rows // 2, width, vectors), jnp.bfloat16)] * 2,
    )(sends, tangent)


def substep_kernel(cols_ref, count_ref, sends_ref, own_hbm, low_hbm, high_hbm, blocks_ref, state_ref,
                   new_state_ref, out_ref, *rest, nnz, per_step, last):
    if last:
        extended, sems = rest
    else:
        to_lower_ref, to_upper_ref, extended, sems = rest
    step = pl.program_id(0)
    slots = own_hbm.shape[0]
    halo = low_hbm.shape[0]

    @pl.when(step == 0)
    def _():
        copies = [
            pltpu.make_async_copy(own_hbm, extended.at[pl.ds(0, slots)], sems.at[0]),
            pltpu.make_async_copy(low_hbm, extended.at[pl.ds(slots, halo)], sems.at[1]),
            pltpu.make_async_copy(high_hbm, extended.at[pl.ds(slots + halo, halo)], sems.at[2]),
        ]
        for copy in copies:
            copy.start()
        for copy in copies:
            copy.wait()

    count = count_ref[0]
    for r in range(per_step):
        row = step * per_step + r
        acc = jnp.zeros(state_ref.shape[1:], jnp.float32)
        for k in range(nnz):
            col = cols_ref[row * nnz + k]
            acc = acc + jnp.dot(blocks_ref[r, k], extended[col], preferred_element_type=jnp.float32)
        new = state_ref[r] + jnp.where(row < count, acc, 0.0)
        new_state_ref[r] = new
        if not last:
            out_ref[r] = new.astype(jnp.bfloat16)
            continue
        part = lax.dot_general(new, new, (((0,), (0,)), ((), ())), precision=lax.Precision.HIGHEST,
                               preferred_element_type=jnp.float32)
        if r == 0:
            @pl.when(step == 0)
            def _():
                out_ref[...] = jnp.zeros_like(out_ref)
        out_ref[...] += part
    if last:
        return
    half = to_lower_ref.shape[0]
    for j in range(2 * half):
        local = sends_ref[j] - step * per_step

        @pl.when((local >= 0) & (local < per_step))
        def _():
            if j < half:
                to_lower_ref[j] = out_ref[local]
            else:
                to_upper_ref[j - half] = out_ref[local]


def substep(cols, count, sends, rounded, from_lower, from_upper, blocks, state, last):
    slots, width, vectors = state.shape
    nnz = blocks.shape[1]
    halo = from_lower.shape[0]
    per_step = ROWS_PER_STEP
    kernel = functools.partial(substep_kernel, nnz=nnz, per_step=per_step, last=last)
    grid_spec = pltpu.PrefetchScalarGridSpec(
        num_scalar_prefetch=3,
        grid=(slots // per_step,),
        in_specs=[
            pl.BlockSpec(memory_space=pl.ANY),
            pl.BlockSpec(memory_space=pl.ANY),
            pl.BlockSpec(memory_space=pl.ANY),
            pl.BlockSpec((per_step, nnz, width, width), lambda i, c, n, q: (i, 0, 0, 0)),
            pl.BlockSpec((per_step, width, vectors), lambda i, c, n, q: (i, 0, 0)),
        ],
        out_specs=[
            pl.BlockSpec((per_step, width, vectors), lambda i, c, n, q: (i, 0, 0)),
            pl.BlockSpec((vectors, vectors), lambda i, c, n, q: (0, 0)) if last
            else pl.BlockSpec((per_step, width, vectors), lambda i, c, n, q: (i, 0, 0)),
        ] + ([] if last else [pl.BlockSpec((halo, width, vectors), lambda i, c, n, q: (0, 0, 0))] * 2),
        scratch_shapes=[
            pltpu.VMEM((slots + 2 * halo, width, vectors), jnp.bfloat16),
            pltpu.SemaphoreType.DMA((3,)),
        ],
    )
    return pl.pallas_call(
        kernel,
        grid_spec=grid_spec,
        out_shape=[
            jax.ShapeDtypeStruct(state.shape, jnp.float32),
            jax.ShapeDtypeStruct((vectors, vectors), jnp.float32) if last
            else jax.ShapeDtypeStruct(state.shape, jnp.bfloat16),
        ] + ([] if last else [jax.ShapeDtypeStruct((halo, width, vectors), jnp.bfloat16)] * 2),
        compiler_params=pltpu.CompilerParams(dimension_semantics=("arbitrary",)),
    )(cols, count, sends, rounded, from_lower, from_upper, blocks, state)


def local(tangent, blocks, columns, counts, send_lists):
    slots, width, vectors = tangent.shape
    live = (jnp.arange(slots, dtype=jnp.int32) < counts[0]).astype(jnp.float32)[:, None, None]
    state = tangent * live
    rounded = state.astype(jnp.bfloat16)
    cols = columns.reshape(-1)
    sends = send_lists.reshape(-1)
    to_lower, to_upper = pick_rows(sends, tangent)
    for step in range(SUBSTEPS):
        from_lower = passed_along(to_upper, "grains", 1)
        from_upper = passed_along(to_lower, "grains", -1)
        if step < SUBSTEPS - 1:
            state, rounded, to_lower, to_upper = substep(
                cols, counts, sends, rounded, from_lower, from_upper, blocks, state, False)
        else:
            state, gram = substep(cols, counts, sends, rounded, from_lower, from_upper, blocks, state, True)
    flat = state.reshape(slots * width, vectors)
    first_low = jnp.linalg.cholesky(tree_sum(gram, "grains"))
    inverse = lax.linalg.triangular_solve(
        first_low, jnp.eye(vectors, dtype=jnp.float32), left_side=True, lower=True
    )
    basis = jnp.dot(flat, inverse.T, precision=lax.Precision.HIGHEST)
    r_factor = first_low.T
    return (basis.reshape(slots, width, vectors), r_factor)


def solution(mesh):
    in_specs = (
        P("grains", None, None),
        P("grains", None, None, None),
        P("grains", None),
        P("grains"),
        P("grains", None, None),
    )
    out_specs = (P("grains", None, None), P())
    return jax.shard_map(local, mesh=mesh, in_specs=in_specs, out_specs=out_specs, check_vma=False)
```

```python
import functools

import jax
import jax.numpy as jnp
from jax import lax
from jax.experimental import pallas as pl
from jax.experimental.pallas import tpu as pltpu
from jax.sharding import PartitionSpec as P

SUBSTEPS = 3
ROWS_PER_STEP = 16


def passed_along(shard, axis, by):
    length = lax.axis_size(axis)
    return lax.ppermute(shard, axis, [(i, (i + by) % length) for i in range(length)])


def tree_sum(value, axis):
    length = lax.axis_size(axis)
    masks = [1]
    bit = 2
    while bit < length:
        masks += [bit, 3 * bit] if 4 * bit <= length else [bit]
        bit *= 4
    for mask in masks:
        partner = [(i, i ^ mask) for i in range(length)]
        value = value + lax.ppermute(value, axis, partner)
    return value


def pick_kernel(sends_ref, tangent_hbm, to_lower_ref, to_upper_ref, buf, sems):
    rows = buf.shape[0]
    half = rows // 2
    copies = [pltpu.make_async_copy(tangent_hbm.at[sends_ref[0, j // half, j % half]], buf.at[j], sems.at[j])
              for j in range(rows)]
    for copy in copies:
        copy.start()
    for j in range(rows):
        copies[j].wait()
        if j < half:
            to_lower_ref[j] = buf[j].astype(jnp.bfloat16)
        else:
            to_upper_ref[j - half] = buf[j].astype(jnp.bfloat16)


def pick_rows(sends, tangent):
    rows = sends.shape[1] * sends.shape[2]
    slots, width, vectors = tangent.shape
    grid_spec = pltpu.PrefetchScalarGridSpec(
        num_scalar_prefetch=1,
        grid=(),
        in_specs=[pl.BlockSpec(memory_space=pl.ANY)],
        out_specs=[pl.BlockSpec(memory_space=pltpu.VMEM)] * 2,
        scratch_shapes=[pltpu.VMEM((rows, width, vectors), jnp.float32), pltpu.SemaphoreType.DMA((rows,))],
    )
    return pl.pallas_call(
        pick_kernel,
        grid_spec=grid_spec,
        out_shape=[jax.ShapeDtypeStruct((rows // 2, width, vectors), jnp.bfloat16)] * 2,
    )(sends, tangent)


def substep_kernel(cols_ref, count_ref, sends_ref, own_hbm, low_hbm, high_hbm, blocks_ref, state_ref,
                   new_state_ref, out_ref, *rest, nnz, per_step, last):
    if last:
        extended, sems = rest
    else:
        to_lower_ref, to_upper_ref, extended, sems = rest
    step = pl.program_id(0)
    slots = own_hbm.shape[0]
    halo = low_hbm.shape[0]

    @pl.when(step == 0)
    def _():
        copies = [
            pltpu.make_async_copy(own_hbm, extended.at[pl.ds(0, slots)], sems.at[0]),
            pltpu.make_async_copy(low_hbm, extended.at[pl.ds(slots, halo)], sems.at[1]),
            pltpu.make_async_copy(high_hbm, extended.at[pl.ds(slots + halo, halo)], sems.at[2]),
        ]
        for copy in copies:
            copy.start()
        for copy in copies:
            copy.wait()

    count = count_ref[0]
    for r in range(per_step):
        row = step * per_step + r
        acc = jnp.zeros(state_ref.shape[1:], jnp.float32)
        for k in range(nnz):
            col = cols_ref[row * nnz + k]
            acc = acc + jnp.dot(blocks_ref[r, k], extended[col], preferred_element_type=jnp.float32)
        new = jnp.where(row < count, state_ref[r] + acc, 0.0)
        new_state_ref[r] = new
        if not last:
            out_ref[r] = new.astype(jnp.bfloat16)
            continue
        part = lax.dot_general(new, new, (((0,), (0,)), ((), ())), precision=lax.Precision.HIGHEST,
                               preferred_element_type=jnp.float32)
        if r == 0:
            @pl.when(step == 0)
            def _():
                out_ref[...] = jnp.zeros_like(out_ref)
        out_ref[...] += part
    if last:
        return
    half = to_lower_ref.shape[0]
    for j in range(2 * half):
        local = sends_ref[0, j // half, j % half] - step * per_step

        @pl.when((local >= 0) & (local < per_step))
        def _():
            if j < half:
                to_lower_ref[j] = out_ref[local]
            else:
                to_upper_ref[j - half] = out_ref[local]


def substep(cols, count, sends, rounded, from_lower, from_upper, blocks, state, last):
    slots, width, vectors = state.shape
    nnz = blocks.shape[1]
    halo = from_lower.shape[0]
    per_step = ROWS_PER_STEP
    kernel = functools.partial(substep_kernel, nnz=nnz, per_step=per_step, last=last)
    grid_spec = pltpu.PrefetchScalarGridSpec(
        num_scalar_prefetch=3,
        grid=(slots // per_step,),
        in_specs=[
            pl.BlockSpec(memory_space=pl.ANY),
            pl.BlockSpec(memory_space=pl.ANY),
            pl.BlockSpec(memory_space=pl.ANY),
            pl.BlockSpec((per_step, nnz, width, width), lambda i, c, n, q: (i, 0, 0, 0)),
            pl.BlockSpec((per_step, width, vectors), lambda i, c, n, q: (i, 0, 0)),
        ],
        out_specs=[
            pl.BlockSpec((per_step, width, vectors), lambda i, c, n, q: (i, 0, 0)),
            pl.BlockSpec((vectors, vectors), lambda i, c, n, q: (0, 0)) if last
            else pl.BlockSpec((per_step, width, vectors), lambda i, c, n, q: (i, 0, 0)),
        ] + ([] if last else [pl.BlockSpec((halo, width, vectors), lambda i, c, n, q: (0, 0, 0))] * 2),
        scratch_shapes=[
            pltpu.VMEM((slots + 2 * halo, width, vectors), jnp.bfloat16),
            pltpu.SemaphoreType.DMA((3,)),
        ],
    )
    return pl.pallas_call(
        kernel,
        grid_spec=grid_spec,
        out_shape=[
            jax.ShapeDtypeStruct(state.shape, jnp.float32),
            jax.ShapeDtypeStruct((vectors, vectors), jnp.float32) if last
            else jax.ShapeDtypeStruct(state.shape, jnp.bfloat16),
        ] + ([] if last else [jax.ShapeDtypeStruct((halo, width, vectors), jnp.bfloat16)] * 2),
        compiler_params=pltpu.CompilerParams(dimension_semantics=("arbitrary",)),
    )(cols, count, sends, rounded, from_lower, from_upper, blocks, state)


def local(tangent, blocks, columns, counts, send_lists):
    slots, width, vectors = tangent.shape
    live = (jnp.arange(slots, dtype=jnp.int32) < counts[0]).astype(jnp.float32)[:, None, None]
    state = tangent
    rounded = (tangent * live).astype(jnp.bfloat16)
    cols = columns.reshape(-1)
    sends = send_lists
    to_lower, to_upper = pick_rows(sends, tangent)
    for step in range(SUBSTEPS):
        from_lower = passed_along(to_upper, "grains", 1)
        from_upper = passed_along(to_lower, "grains", -1)
        if step < SUBSTEPS - 1:
            state, rounded, to_lower, to_upper = substep(
                cols, counts, sends, rounded, from_lower, from_upper, blocks, state, False)
        else:
            state, gram = substep(cols, counts, sends, rounded, from_lower, from_upper, blocks, state, True)
    flat = state.reshape(slots * width, vectors)
    first_low = lax.linalg.cholesky(tree_sum(gram, "grains"), symmetrize_input=False)
    inverse = lax.linalg.triangular_solve(
        first_low, jnp.eye(vectors, dtype=jnp.float32), left_side=True, lower=True
    )
    basis = jnp.dot(flat, inverse.T, precision=lax.Precision.HIGHEST)
    r_factor = first_low.T
    return (basis.reshape(slots, width, vectors), r_factor)


def solution(mesh):
    in_specs = (
        P("grains", None, None),
        P("grains", None, None, None),
        P("grains", None),
        P("grains"),
        P("grains", None, None),
    )
    out_specs = (P("grains", None, None), P())
    return jax.shard_map(local, mesh=mesh, in_specs=in_specs, out_specs=out_specs, check_vma=False)
```

```python
import functools

import jax
import jax.numpy as jnp
from jax import lax
from jax.experimental import pallas as pl
from jax.experimental.pallas import tpu as pltpu
from jax.sharding import PartitionSpec as P

SUBSTEPS = 3
ROWS_PER_STEP = 16


def passed_along(shard, axis, by):
    length = lax.axis_size(axis)
    return lax.ppermute(shard, axis, [(i, (i + by) % length) for i in range(length)])


def tree_sum(value, axis):
    length = lax.axis_size(axis)
    masks = [1]
    bit = 2
    while bit < length:
        masks += [bit, 3 * bit] if 4 * bit <= length else [bit]
        bit *= 4
    for mask in masks:
        partner = [(i, i ^ mask) for i in range(length)]
        value = value + lax.ppermute(value, axis, partner)
    return value


def pick_kernel(sends_ref, tangent_hbm, to_lower_ref, to_upper_ref, buf, sems):
    rows = buf.shape[0]
    half = rows // 2
    copies = [pltpu.make_async_copy(tangent_hbm.at[sends_ref[0, j // half, j % half]], buf.at[j], sems.at[j])
              for j in range(rows)]
    for copy in copies:
        copy.start()
    for j in range(rows):
        copies[j].wait()
        if j < half:
            to_lower_ref[j] = buf[j].astype(jnp.bfloat16)
        else:
            to_upper_ref[j - half] = buf[j].astype(jnp.bfloat16)


def pick_rows(sends, tangent):
    rows = sends.shape[1] * sends.shape[2]
    slots, width, vectors = tangent.shape
    grid_spec = pltpu.PrefetchScalarGridSpec(
        num_scalar_prefetch=1,
        grid=(),
        in_specs=[pl.BlockSpec(memory_space=pl.ANY)],
        out_specs=[pl.BlockSpec(memory_space=pltpu.VMEM)] * 2,
        scratch_shapes=[pltpu.VMEM((rows, width, vectors), jnp.float32), pltpu.SemaphoreType.DMA((rows,))],
    )
    return pl.pallas_call(
        pick_kernel,
        grid_spec=grid_spec,
        out_shape=[jax.ShapeDtypeStruct((rows // 2, width, vectors), jnp.bfloat16)] * 2,
    )(sends, tangent)


def substep_kernel(cols_ref, count_ref, sends_ref, own_hbm, low_hbm, high_hbm, blocks_ref, state_ref,
                   new_state_ref, out_ref, *rest, nnz, per_step, last):
    if last:
        extended, sems = rest
    else:
        to_lower_ref, to_upper_ref, extended, sems = rest
    step = pl.program_id(0)
    slots = own_hbm.shape[0]
    halo = low_hbm.shape[0]

    @pl.when(step == 0)
    def _():
        copies = [
            pltpu.make_async_copy(own_hbm, extended.at[pl.ds(0, slots)], sems.at[0]),
            pltpu.make_async_copy(low_hbm, extended.at[pl.ds(slots, halo)], sems.at[1]),
            pltpu.make_async_copy(high_hbm, extended.at[pl.ds(slots + halo, halo)], sems.at[2]),
        ]
        for copy in copies:
            copy.start()
        for copy in copies:
            copy.wait()

    count = count_ref[0]
    for r in range(per_step):
        row = step * per_step + r
        acc = jnp.zeros(state_ref.shape[1:], jnp.float32)
        for k in range(nnz):
            col = cols_ref[row * nnz + k]
            acc = acc + jnp.dot(blocks_ref[r, k], extended[col], preferred_element_type=jnp.float32)
        new = jnp.where(row < count, state_ref[r] + acc, 0.0)
        new_state_ref[r] = new
        if not last:
            out_ref[r] = new.astype(jnp.bfloat16)
            continue
        part = lax.dot_general(new, new, (((0,), (0,)), ((), ())), precision=lax.Precision.HIGHEST,
                               preferred_element_type=jnp.float32)
        if r == 0:
            @pl.when(step == 0)
            def _():
                out_ref[...] = jnp.zeros_like(out_ref)
        out_ref[...] += part
    if last:
        return
    half = to_lower_ref.shape[0]
    for j in range(2 * half):
        local = sends_ref[0, j // half, j % half] - step * per_step

        @pl.when((local >= 0) & (local < per_step))
        def _():
            if j < half:
                to_lower_ref[j] = out_ref[local]
            else:
                to_upper_ref[j - half] = out_ref[local]


def substep(cols, count, sends, rounded, from_lower, from_upper, blocks, state, last):
    slots, width, vectors = state.shape
    nnz = blocks.shape[1]
    halo = from_lower.shape[0]
    per_step = ROWS_PER_STEP
    kernel = functools.partial(substep_kernel, nnz=nnz, per_step=per_step, last=last)
    grid_spec = pltpu.PrefetchScalarGridSpec(
        num_scalar_prefetch=3,
        grid=(slots // per_step,),
        in_specs=[
            pl.BlockSpec(memory_space=pl.ANY),
            pl.BlockSpec(memory_space=pl.ANY),
            pl.BlockSpec(memory_space=pl.ANY),
            pl.BlockSpec((per_step, nnz, width, width), lambda i, c, n, q: (i, 0, 0, 0)),
            pl.BlockSpec((per_step, width, vectors), lambda i, c, n, q: (i, 0, 0)),
        ],
        out_specs=[
            pl.BlockSpec((per_step, width, vectors), lambda i, c, n, q: (i, 0, 0)),
            pl.BlockSpec((vectors, vectors), lambda i, c, n, q: (0, 0)) if last
            else pl.BlockSpec((per_step, width, vectors), lambda i, c, n, q: (i, 0, 0)),
        ] + ([] if last else [pl.BlockSpec((halo, width, vectors), lambda i, c, n, q: (0, 0, 0))] * 2),
        scratch_shapes=[
            pltpu.VMEM((slots + 2 * halo, width, vectors), jnp.bfloat16),
            pltpu.SemaphoreType.DMA((3,)),
        ],
    )
    return pl.pallas_call(
        kernel,
        grid_spec=grid_spec,
        out_shape=[
            jax.ShapeDtypeStruct(state.shape, jnp.float32),
            jax.ShapeDtypeStruct((vectors, vectors), jnp.float32) if last
            else jax.ShapeDtypeStruct(state.shape, jnp.bfloat16),
        ] + ([] if last else [jax.ShapeDtypeStruct((halo, width, vectors), jnp.bfloat16)] * 2),
        compiler_params=pltpu.CompilerParams(dimension_semantics=("arbitrary",)),
    )(cols, count, sends, rounded, from_lower, from_upper, blocks, state)


def local(tangent, blocks, columns, counts, send_lists):
    slots, width, vectors = tangent.shape
    live = (jnp.arange(slots, dtype=jnp.int32) < counts[0]).astype(jnp.float32)[:, None, None]
    state = tangent
    rounded = (tangent * live).astype(jnp.bfloat16)
    cols = columns.reshape(-1)
    sends = send_lists
    to_lower, to_upper = pick_rows(sends, tangent)
    for step in range(SUBSTEPS):
        from_lower = passed_along(to_upper, "grains", 1)
        from_upper = passed_along(to_lower, "grains", -1)
        if step < SUBSTEPS - 1:
            state, rounded, to_lower, to_upper = substep(
                cols, counts, sends, rounded, from_lower, from_upper, blocks, state, False)
        else:
            state, gram = substep(cols, counts, sends, rounded, from_lower, from_upper, blocks, state, True)
    flat = state.reshape(slots * width, vectors)
    first_low = lax.linalg.cholesky(tree_sum(gram, "grains"), symmetrize_input=False)
    inverse_t = lax.linalg.triangular_solve(
        first_low, jnp.eye(vectors, dtype=jnp.float32), left_side=True, lower=True, transpose_a=True
    )
    basis = jnp.dot(flat, inverse_t, precision=lax.Precision.HIGHEST)
    r_factor = first_low.T
    return (basis.reshape(slots, width, vectors), r_factor)


def solution(mesh):
    in_specs = (
        P("grains", None, None),
        P("grains", None, None, None),
        P("grains", None),
        P("grains"),
        P("grains", None, None),
    )
    out_specs = (P("grains", None, None), P())
    return jax.shard_map(local, mesh=mesh, in_specs=in_specs, out_specs=out_specs, check_vma=False)
```

```python
import functools

import jax
import jax.numpy as jnp
from jax import lax
from jax.experimental import pallas as pl
from jax.experimental.pallas import tpu as pltpu
from jax.sharding import PartitionSpec as P

SUBSTEPS = 3
ROWS_PER_STEP = 16


def passed_along(shard, axis, by):
    length = lax.axis_size(axis)
    return lax.ppermute(shard, axis, [(i, (i + by) % length) for i in range(length)])


def tree_sum(value, axis):
    length = lax.axis_size(axis)
    masks = [1]
    bit = 2
    while bit < length:
        masks += [bit, 3 * bit] if 4 * bit <= length else [bit]
        bit *= 4
    for mask in masks:
        partner = [(i, i ^ mask) for i in range(length)]
        value = value + lax.ppermute(value, axis, partner)
    return value


def pick_kernel(sends_ref, tangent_hbm, to_lower_ref, to_upper_ref, buf, sems):
    rows = buf.shape[0]
    half = rows // 2
    copies = [pltpu.make_async_copy(tangent_hbm.at[sends_ref[0, j // half, j % half]], buf.at[j], sems.at[j])
              for j in range(rows)]
    for copy in copies:
        copy.start()
    for j in range(rows):
        copies[j].wait()
        if j < half:
            to_lower_ref[j] = buf[j].astype(jnp.bfloat16)
        else:
            to_upper_ref[j - half] = buf[j].astype(jnp.bfloat16)


def pick_rows(sends, tangent):
    rows = sends.shape[1] * sends.shape[2]
    slots, width, vectors = tangent.shape
    grid_spec = pltpu.PrefetchScalarGridSpec(
        num_scalar_prefetch=1,
        grid=(),
        in_specs=[pl.BlockSpec(memory_space=pl.ANY)],
        out_specs=[pl.BlockSpec(memory_space=pltpu.VMEM)] * 2,
        scratch_shapes=[pltpu.VMEM((rows, width, vectors), jnp.float32), pltpu.SemaphoreType.DMA((rows,))],
    )
    return pl.pallas_call(
        pick_kernel,
        grid_spec=grid_spec,
        out_shape=[jax.ShapeDtypeStruct((rows // 2, width, vectors), jnp.bfloat16)] * 2,
    )(sends, tangent)


def substep_kernel(cols_ref, count_ref, sends_ref, own_hbm, low_hbm, high_hbm, blocks_ref, state_ref,
                   new_state_ref, out_ref, *rest, nnz, per_step, last):
    if last:
        extended, sems = rest
    else:
        to_lower_ref, to_upper_ref, extended, sems = rest
    step = pl.program_id(0)
    slots = own_hbm.shape[0]
    halo = low_hbm.shape[0]

    @pl.when(step == 0)
    def _():
        copies = [
            pltpu.make_async_copy(own_hbm, extended.at[pl.ds(0, slots)], sems.at[0]),
            pltpu.make_async_copy(low_hbm, extended.at[pl.ds(slots, halo)], sems.at[1]),
            pltpu.make_async_copy(high_hbm, extended.at[pl.ds(slots + halo, halo)], sems.at[2]),
        ]
        for copy in copies:
            copy.start()
        for copy in copies:
            copy.wait()

    count = count_ref[0]
    gram = None
    for r in range(per_step):
        row = step * per_step + r
        acc = jnp.zeros(state_ref.shape[1:], jnp.float32)
        for k in range(nnz):
            col = cols_ref[row * nnz + k]
            acc = acc + jnp.dot(blocks_ref[r, k], extended[col], preferred_element_type=jnp.float32)
        new = jnp.where(row < count, state_ref[r] + acc, 0.0)
        new_state_ref[r] = new
        if not last:
            out_ref[r] = new.astype(jnp.bfloat16)
            continue
        part = lax.dot_general(new, new, (((0,), (0,)), ((), ())), precision=lax.Precision.HIGHEST,
                               preferred_element_type=jnp.float32)
        gram = part if gram is None else gram + part
    if last:
        @pl.when(step == 0)
        def _():
            out_ref[...] = jnp.zeros_like(out_ref)

        out_ref[...] += gram
        return
    half = to_lower_ref.shape[0]
    for j in range(2 * half):
        local = sends_ref[0, j // half, j % half] - step * per_step

        @pl.when((local >= 0) & (local < per_step))
        def _():
            if j < half:
                to_lower_ref[j] = out_ref[local]
            else:
                to_upper_ref[j - half] = out_ref[local]


def substep(cols, count, sends, rounded, from_lower, from_upper, blocks, state, last):
    slots, width, vectors = state.shape
    nnz = blocks.shape[1]
    halo = from_lower.shape[0]
    per_step = ROWS_PER_STEP
    kernel = functools.partial(substep_kernel, nnz=nnz, per_step=per_step, last=last)
    grid_spec = pltpu.PrefetchScalarGridSpec(
        num_scalar_prefetch=3,
        grid=(slots // per_step,),
        in_specs=[
            pl.BlockSpec(memory_space=pl.ANY),
            pl.BlockSpec(memory_space=pl.ANY),
            pl.BlockSpec(memory_space=pl.ANY),
            pl.BlockSpec((per_step, nnz, width, width), lambda i, c, n, q: (i, 0, 0, 0)),
            pl.BlockSpec((per_step, width, vectors), lambda i, c, n, q: (i, 0, 0)),
        ],
        out_specs=[
            pl.BlockSpec((per_step, width, vectors), lambda i, c, n, q: (i, 0, 0)),
            pl.BlockSpec((vectors, vectors), lambda i, c, n, q: (0, 0)) if last
            else pl.BlockSpec((per_step, width, vectors), lambda i, c, n, q: (i, 0, 0)),
        ] + ([] if last else [pl.BlockSpec((halo, width, vectors), lambda i, c, n, q: (0, 0, 0))] * 2),
        scratch_shapes=[
            pltpu.VMEM((slots + 2 * halo, width, vectors), jnp.bfloat16),
            pltpu.SemaphoreType.DMA((3,)),
        ],
    )
    return pl.pallas_call(
        kernel,
        grid_spec=grid_spec,
        out_shape=[
            jax.ShapeDtypeStruct(state.shape, jnp.float32),
            jax.ShapeDtypeStruct((vectors, vectors), jnp.float32) if last
            else jax.ShapeDtypeStruct(state.shape, jnp.bfloat16),
        ] + ([] if last else [jax.ShapeDtypeStruct((halo, width, vectors), jnp.bfloat16)] * 2),
        compiler_params=pltpu.CompilerParams(dimension_semantics=("arbitrary",)),
    )(cols, count, sends, rounded, from_lower, from_upper, blocks, state)


def local(tangent, blocks, columns, counts, send_lists):
    slots, width, vectors = tangent.shape
    live = (jnp.arange(slots, dtype=jnp.int32) < counts[0]).astype(jnp.float32)[:, None, None]
    state = tangent
    rounded = (tangent * live).astype(jnp.bfloat16)
    cols = columns.reshape(-1)
    sends = send_lists
    to_lower, to_upper = pick_rows(sends, tangent)
    for step in range(SUBSTEPS):
        from_lower = passed_along(to_upper, "grains", 1)
        from_upper = passed_along(to_lower, "grains", -1)
        if step < SUBSTEPS - 1:
            state, rounded, to_lower, to_upper = substep(
                cols, counts, sends, rounded, from_lower, from_upper, blocks, state, False)
        else:
            state, gram = substep(cols, counts, sends, rounded, from_lower, from_upper, blocks, state, True)
    flat = state.reshape(slots * width, vectors)
    first_low = lax.linalg.cholesky(tree_sum(gram, "grains"), symmetrize_input=False)
    inverse = lax.linalg.triangular_solve(
        first_low, jnp.eye(vectors, dtype=jnp.float32), left_side=True, lower=True
    )
    basis = jnp.dot(flat, inverse.T, precision=lax.Precision.HIGHEST)
    r_factor = first_low.T
    return (basis.reshape(slots, width, vectors), r_factor)


def solution(mesh):
    in_specs = (
        P("grains", None, None),
        P("grains", None, None, None),
        P("grains", None),
        P("grains"),
        P("grains", None, None),
    )
    out_specs = (P("grains", None, None), P())
    return jax.shard_map(local, mesh=mesh, in_specs=in_specs, out_specs=out_specs, check_vma=False)
```
